1024 devices in a mesh: ctx: 64 (over z, x), head: 16 (over y, core).
Axes of the slice: x: 4, y: 8, z: 16, core: 2. Of those that a mesh axis runs over, the one named last changes fastest.
Arguments:
- q_raw: bfloat16 [16384, 2048], P('ctx', 'head'), may hold values from -6 to 6
- k_raw: bfloat16 [16384, 2048], P('ctx', 'head'), may hold values from -6 to 6
- v_raw: bfloat16 [16384, 2048], P('ctx', 'head'), may hold values from -6 to 6
- conv_weight: float32 [3, 4, 2048], P(None, None, 'head'), may hold values from -3 to 3
- beta_logit: float32 [16, 16384], P('head', 'ctx'), may hold values from -10 to 3.5
- out_weight: bfloat16 [2048, 2048], P('head'), may hold values from -0.125 to 0.125
- out_grad: bfloat16 [16384, 2048], P('ctx', 'head'), may hold values from -6 to 6
Outputs:
- grad_q_raw: float32 [16384, 2048], P('ctx', 'head')
- grad_k_raw: float32 [16384, 2048], P('ctx', 'head')
- grad_v_raw: float32 [16384, 2048], P('ctx', 'head')
- grad_conv: float32 [3, 4, 2048], P(None, None, 'head')
- grad_beta: float32 [16, 16384], P('head', 'ctx')
The draws below stay inside these ranges and needn't reach their ends.
All inputs are finite; a program needn't handle non-finite values.
Results may differ from the reference program's by a relative error of at most 0.00095.
Values may be sent and summed in bfloat16 or wider, within the bound.
No kernel may reach another device: no remote copies, remote signals or barrier semaphores. Data moves between devices by JAX's collectives and lax.ppermute only.
A program may use at most 64 MiB of HBM per device.

```python
import math
import jax
import jax.numpy as jnp
from jax import lax

D = 2048
FEATURE_DIM = 128
CONV = 4
BLOCK = 64
TOK_DEV = 256
ATTENTION_GROUPS = 16
SEQUENCE_STEPS = 16384


def draw_beta_logit(key, part):
    lookup_feature_rows = jax.random.split(key, 6)
    share = 0.5
    slow = jax.random.uniform(lookup_feature_rows[0], (ATTENTION_GROUPS, 1)) < share
    slow_rate = jnp.exp(jax.random.uniform(lookup_feature_rows[1], (ATTENTION_GROUPS, 1), minval=math.log(64.0), maxval=math.log(256.0))) / SEQUENCE_STEPS
    slow_rate = jnp.minimum(slow_rate, 0.2)
    fast_rate = jax.random.uniform(lookup_feature_rows[2], (ATTENTION_GROUPS, 1), minval=0.3, maxval=0.9)
    base = jnp.where(slow, slow_rate, fast_rate)
    rough = jnp.exp(jax.random.uniform(lookup_feature_rows[3], (ATTENTION_GROUPS, SEQUENCE_STEPS), minval=math.log(0.5), maxval=math.log(2.0)))
    device_count = SEQUENCE_STEPS // TOK_DEV
    device_factor = jnp.exp(jax.random.uniform(lookup_feature_rows[4], (ATTENTION_GROUPS, device_count, 1), minval=math.log(0.5), maxval=math.log(2.0)))
    device_factor = jnp.broadcast_to(device_factor, (ATTENTION_GROUPS, device_count, TOK_DEV)).reshape(ATTENTION_GROUPS, SEQUENCE_STEPS)
    rate = base * rough * device_factor
    segment_span = FEATURE_DIM // 2
    segment_leading_index = jax.random.randint(lookup_feature_rows[5], (ATTENTION_GROUPS, 4, 1), 0, SEQUENCE_STEPS - segment_span + 1)
    sequence_indices = jnp.arange(SEQUENCE_STEPS, dtype=jnp.int32)[None, None, :]
    within_segment_offset = jnp.any((sequence_indices >= segment_leading_index) & (sequence_indices < segment_leading_index + segment_span), axis=1)
    rate = jnp.where(slow & within_segment_offset, 0.9, rate)
    rate = jnp.minimum(rate, 0.97).astype(jnp.float32)
    return (jnp.log(rate) - jnp.log1p(-rate)).astype(jnp.float32)


def shard_levels(own_key, extent, cuts, low, high):
    def one(dim, shards_of):
        heights = jax.random.uniform(jax.random.fold_in(jax.random.fold_in(own_key, 6), dim), (shards_of,), jnp.float32, low / len(cuts), high / len(cuts))
        return jnp.repeat(jnp.exp(heights), extent[dim] // shards_of).reshape((-1,) + (1,) * (len(extent) - dim - 1))

    level = one(*cuts[0])
    for cut in cuts[1:]:
        level = level * one(*cut)
    return level


def noise(own_key, dims, deviation, limit, cuts=(), kind=jnp.bfloat16):
    gain = shard_levels(own_key, dims, cuts, -0.22, 0.18) if cuts else 1.0
    result = jax.random.normal(own_key, dims, jnp.float32) * deviation * gain
    return jnp.minimum(jnp.maximum(result, -limit), limit).astype(kind)


def setup_inputs(seed: int = 0) -> dict:
    seeds = jax.random.split(jax.random.key(seed), 8)
    q_raw = noise(seeds[0], (SEQUENCE_STEPS, ATTENTION_GROUPS * FEATURE_DIM), 1.0, 6.0, ((0, 64), (1, 16)))
    k_raw = noise(seeds[1], (SEQUENCE_STEPS, ATTENTION_GROUPS * FEATURE_DIM), 1.0, 6.0, ((0, 64), (1, 16)))
    v_raw = noise(seeds[2], (SEQUENCE_STEPS, ATTENTION_GROUPS * FEATURE_DIM), 1.0, 6.0, ((0, 64), (1, 16)))
    conv_weight = noise(seeds[3], (3, CONV, ATTENTION_GROUPS * FEATURE_DIM), CONV ** -0.5, 3.0, ((2, 16),), jnp.float32)
    beta_logit = draw_beta_logit(jax.random.fold_in(seeds[7], 71), 0)
    out_weight = noise(seeds[5], (ATTENTION_GROUPS * FEATURE_DIM, D), (ATTENTION_GROUPS * FEATURE_DIM) ** -0.5, 0.125, ((0, 16),))
    out_grad = noise(seeds[6], (SEQUENCE_STEPS, D), 1.0, 6.0, ((0, 64), (1, 16)))
    return dict(q_raw=q_raw, k_raw=k_raw, v_raw=v_raw, conv_weight=conv_weight, beta_logit=beta_logit, out_weight=out_weight, out_grad=out_grad)


HIGHEST = lax.Precision.HIGHEST

def conv_silu(extended, weights, row_count):
    summed = weights[0] * extended[0:row_count]
    for offset in range(1, CONV):
        summed = summed + weights[offset] * extended[offset:offset + row_count]
    return jax.nn.silu(summed)

def normed(entries):
    return entries * lax.rsqrt(lax.optimization_barrier(jnp.sum(entries * entries, axis=-1, keepdims=True)) + 1e-06)

def wy_factors(key_rows, value_rows, rates):
    weighted = key_rows * rates[:, None]
    strict = jnp.tril(jnp.dot(weighted, key_rows.T, precision=HIGHEST), -1)
    system = jnp.eye(strict.shape[0], dtype=strict.dtype) + strict
    w_keys = jax.scipy.linalg.solve_triangular(system, weighted, lower=True, unit_diagonal=True)
    w_values = jax.scipy.linalg.solve_triangular(system, value_rows * rates[:, None], lower=True, unit_diagonal=True)
    return (w_keys, w_values)

def block_step(state, block):
    query_rows, key_rows, value_rows, rates = block
    w_keys, w_values = wy_factors(key_rows, value_rows, rates)
    fresh = w_values - jnp.dot(w_keys, state, precision=HIGHEST)
    scores = jnp.tril(jnp.dot(query_rows, key_rows.T, precision=HIGHEST))
    output = jnp.dot(query_rows, state, precision=HIGHEST) + jnp.dot(scores, fresh, precision=HIGHEST)
    return (state + jnp.dot(key_rows.T, fresh, precision=HIGHEST), output)

def head_forward(raw_q, raw_k, raw_v, conv_three, logits):
    row_count = raw_q.shape[0]
    padding = jnp.zeros((CONV - 1, FEATURE_DIM), raw_q.dtype)

    def activate(raw_rows, which_conv):
        return conv_silu(jnp.concatenate([padding, raw_rows], 0), conv_three[which_conv], row_count)
    queries = normed(activate(raw_q, 0))
    key_act = normed(activate(raw_k, 1))
    value_act = activate(raw_v, 2)
    rates = jax.nn.sigmoid(logits)
    blocks = row_count // BLOCK
    shaped = (queries.reshape(blocks, BLOCK, FEATURE_DIM), key_act.reshape(blocks, BLOCK, FEATURE_DIM), value_act.reshape(blocks, BLOCK, FEATURE_DIM), rates.reshape(blocks, BLOCK))
    _, outputs = lax.scan(block_step, jnp.zeros((FEATURE_DIM, FEATURE_DIM), raw_q.dtype), shaped)
    return outputs.reshape(row_count, FEATURE_DIM)

def reference(q_raw, k_raw, v_raw, conv_weight, beta_logit, out_weight, out_grad):

    def one_head(head_index):
        start = head_index * FEATURE_DIM

        def columns(array):
            return lax.dynamic_slice_in_dim(array, start, FEATURE_DIM, 1).astype(jnp.float32)
        conv_three = lax.dynamic_slice_in_dim(conv_weight, start, FEATURE_DIM, 2)
        logits = lax.dynamic_index_in_dim(beta_logit, head_index, 0, keepdims=False)
        weight_rows = lax.dynamic_slice_in_dim(out_weight, start, FEATURE_DIM, 0)
        out_cot = jnp.dot(out_grad.astype(jnp.float32), weight_rows.T.astype(jnp.float32), preferred_element_type=jnp.float32)
        _, backward = jax.vjp(head_forward, columns(q_raw), columns(k_raw), columns(v_raw), conv_three, logits)
        return backward(out_cot)
    grads = lax.map(one_head, jnp.arange(ATTENTION_GROUPS, dtype=jnp.int32))

    def merge_heads(stacked):
        return jnp.transpose(stacked, (1, 0, 2)).reshape(SEQUENCE_STEPS, ATTENTION_GROUPS * FEATURE_DIM)
    grad_conv = jnp.transpose(grads[3], (1, 2, 0, 3)).reshape(3, CONV, ATTENTION_GROUPS * FEATURE_DIM) * (1.0 / math.sqrt(SEQUENCE_STEPS))
    return (merge_heads(grads[0]), merge_heads(grads[1]), merge_heads(grads[2]), grad_conv, grads[4])
```

```python
import math

import jax
import jax.numpy as jnp
from jax import lax
from jax.sharding import PartitionSpec as P

FEATURE_DIM = 128
CONV = 4
BLOCK = 64


HIGHEST = lax.Precision.HIGHEST


def passed_along(block, axis, distance):
    devices = range(lax.axis_size(axis))
    route = [(i - distance, i) for i in devices if i - distance in devices]
    return lax.ppermute(block, axis, route)


def carried_in(parts, axis, combine, identity, reverse):
    count = lax.axis_size(axis)
    place = lax.axis_index(axis)
    ranks = [count - 1 - place if back else place for back in reverse]
    fill = lambda a, e: jnp.zeros_like(a) + jnp.asarray(e, a.dtype)
    totals = list(parts)
    states = [jax.tree.map(fill, part, identity) for part in parts]
    distance = 1
    while distance < count:
        for n, back in enumerate(reverse):
            got = passed_along(totals[n], axis, -distance if back else distance)
            keep = lambda new, old: jnp.where(ranks[n] >= distance, new, old)
            states[n] = jax.tree.map(keep, combine(got, states[n]), states[n])
            if 2 * distance < count:
                totals[n] = jax.tree.map(keep, combine(got, totals[n]), totals[n])
        distance *= 2
    return states


def conv_silu(extended, weights, row_count):
    summed = weights[0] * extended[0:row_count]
    for offset in range(1, CONV):
        summed = summed + weights[offset] * extended[offset : offset + row_count]
    return jax.nn.silu(summed)


def normed(entries):
    return entries * lax.rsqrt(jnp.sum(entries * entries, axis=-1, keepdims=True) + 1e-06)


def wy_factors(key_rows, value_rows, rates):
    weighted = key_rows * rates[:, None]
    strict = jnp.tril(jnp.dot(weighted, key_rows.T, precision=HIGHEST), -1)
    system = jnp.eye(strict.shape[0], dtype=strict.dtype) + strict
    w_keys = jax.scipy.linalg.solve_triangular(system, weighted, lower=True, unit_diagonal=True)
    w_values = jax.scipy.linalg.solve_triangular(
        system, value_rows * rates[:, None], lower=True, unit_diagonal=True
    )
    return (w_keys, w_values)


def block_step(state, block):
    query_rows, key_rows, value_rows, rates = block
    w_keys, w_values = wy_factors(key_rows, value_rows, rates)
    fresh = w_values - jnp.dot(w_keys, state, precision=HIGHEST)
    scores = jnp.tril(jnp.dot(query_rows, key_rows.T, precision=HIGHEST))
    output = jnp.dot(query_rows, state, precision=HIGHEST) + jnp.dot(
        scores, fresh, precision=HIGHEST
    )
    return (state + jnp.dot(key_rows.T, fresh, precision=HIGHEST), output)


def local_forward(ext_q, ext_k, ext_v, conv_three, logits, start_state):
    row_count = logits.shape[0]
    queries = normed(conv_silu(ext_q, conv_three[0], row_count))
    key_act = normed(conv_silu(ext_k, conv_three[1], row_count))
    value_act = conv_silu(ext_v, conv_three[2], row_count)
    rates = jax.nn.sigmoid(logits)
    blocks = row_count // BLOCK
    shaped = (
        queries.reshape(blocks, BLOCK, FEATURE_DIM),
        key_act.reshape(blocks, BLOCK, FEATURE_DIM),
        value_act.reshape(blocks, BLOCK, FEATURE_DIM),
        rates.reshape(blocks, BLOCK),
    )
    final, outputs = lax.scan(block_step, start_state, shaped)
    return (outputs.reshape(row_count, FEATURE_DIM), final)


def transition(ext_k, ext_v, conv_three, logits):
    row_count = logits.shape[0]
    key_act = normed(conv_silu(ext_k, conv_three[1], row_count))
    value_act = conv_silu(ext_v, conv_three[2], row_count)
    rates = jax.nn.sigmoid(logits)
    blocks = row_count // BLOCK
    shaped = (
        key_act.reshape(blocks, BLOCK, FEATURE_DIM),
        value_act.reshape(blocks, BLOCK, FEATURE_DIM),
        rates.reshape(blocks, BLOCK),
    )
    identity = jnp.eye(FEATURE_DIM, dtype=jnp.float32)

    def advance(carry, block):
        key_rows, value_rows, block_rates = block
        w_keys, w_values = wy_factors(key_rows, value_rows, block_rates)
        decay = identity - jnp.dot(key_rows.T, w_keys, precision=HIGHEST)
        written = jnp.dot(key_rows.T, w_values, precision=HIGHEST)
        return (
            (
                jnp.dot(decay, carry[0], precision=HIGHEST),
                jnp.dot(decay, carry[1], precision=HIGHEST) + written,
            ),
            None,
        )

    pairs, _ = lax.scan(
        advance, (identity, jnp.zeros((FEATURE_DIM, FEATURE_DIM), jnp.float32)), shaped
    )
    return pairs


def combine_pairs(earlier, later):
    product = jnp.matmul(later[0], earlier[0], precision=HIGHEST)
    offset_term = jnp.matmul(later[0], earlier[1], precision=HIGHEST) + later[1]
    return (product, offset_term)


def on_device(q_raw, k_raw, v_raw, conv_weight, beta_logit, out_weight, out_grad):
    row_count = q_raw.shape[0]
    col_count = q_raw.shape[1]
    head_count = col_count // FEATURE_DIM
    margin = CONV - 1
    tail = row_count - margin
    rim_rows = passed_along((q_raw[tail:], k_raw[tail:], v_raw[tail:]), "ctx", 1)

    def extend(rim_part, main_part):
        joined = jnp.concatenate([rim_part, main_part], 0).astype(jnp.float32)
        return joined.reshape(margin + row_count, head_count, FEATURE_DIM).transpose(1, 0, 2)

    ext_q = extend(rim_rows[0], q_raw)
    ext_k = extend(rim_rows[1], k_raw)
    ext_v = extend(rim_rows[2], v_raw)
    conv_heads = conv_weight.reshape(3, CONV, head_count, FEATURE_DIM).transpose(2, 0, 1, 3)
    out_cot = lax.dot_general(
        lax.all_gather(out_grad, "head", axis=1, tiled=True),
        out_weight,
        (((1,), (1,)), ((), ())),
        preferred_element_type=jnp.float32,
    )
    out_cot = out_cot.reshape(row_count, head_count, FEATURE_DIM).transpose(1, 0, 2)
    pairs = jax.vmap(transition)(ext_k, ext_v, conv_heads, beta_logit)
    identity = jnp.broadcast_to(
        jnp.eye(FEATURE_DIM, dtype=jnp.float32), (head_count, FEATURE_DIM, FEATURE_DIM)
    )
    zero_state = jnp.zeros((head_count, FEATURE_DIM, FEATURE_DIM), jnp.float32)
    batched = jax.vmap(local_forward)
    adjoint_map = jnp.swapaxes(pairs[0], 1, 2)
    _, seed_backward = jax.vjp(batched, ext_q, ext_k, ext_v, conv_heads, beta_logit, zero_state)
    local_seed = seed_backward((out_cot, zero_state))[5]
    carried, suffix = carried_in(
        [pairs, (adjoint_map, local_seed)],
        "ctx",
        combine_pairs,
        (identity, zero_state),
        [False, True],
    )
    start_state = carried[1]
    _, backward = jax.vjp(batched, ext_q, ext_k, ext_v, conv_heads, beta_logit, start_state)
    grads = backward((out_cot, suffix[1]))
    rim_back = passed_along(
        (grads[0][:, :margin], grads[1][:, :margin], grads[2][:, :margin]), "ctx", -1
    )

    def finish(grad_ext, rim_part):
        main_part = grad_ext[:, margin:]
        main_part = jnp.concatenate([main_part[:, :tail], main_part[:, tail:] + rim_part], 1)
        return main_part.transpose(1, 0, 2).reshape(row_count, col_count)

    conv_local = grads[3].transpose(1, 2, 0, 3).reshape(3, CONV, col_count)
    scale = 1.0 / math.sqrt(row_count * lax.axis_size("ctx"))
    conv_total = lax.psum(conv_local, "ctx") * scale
    return (
        finish(grads[0], rim_back[0]),
        finish(grads[1], rim_back[1]),
        finish(grads[2], rim_back[2]),
        conv_total,
        grads[4],
    )


def solution(mesh):
    return jax.shard_map(
        on_device,
        mesh=mesh,
        in_specs=(
            P("ctx", "head"),
            P("ctx", "head"),
            P("ctx", "head"),
            P(None, None, "head"),
            P("head", "ctx"),
            P("head", None),
            P("ctx", "head"),
        ),
        out_specs=(
            P("ctx", "head"),
            P("ctx", "head"),
            P("ctx", "head"),
            P(None, None, "head"),
            P("head", "ctx"),
        ),
        check_vma=False,
    )
```

```python
import math

import jax
import jax.numpy as jnp
from jax import lax
from jax.sharding import PartitionSpec as P

FEATURE_DIM = 128
CONV = 4
BLOCK = 64


HIGHEST = lax.Precision.HIGHEST


def passed_along(block, axis, distance):
    devices = range(lax.axis_size(axis))
    route = [(i - distance, i) for i in devices if i - distance in devices]
    return lax.ppermute(block, axis, route)


def carried_in(parts, axis, combine, identity, reverse, radix=4):
    count = lax.axis_size(axis)
    place = lax.axis_index(axis)
    ranks = [count - 1 - place if back else place for back in reverse]
    fill = lambda a, e: jnp.zeros_like(a) + jnp.asarray(e, a.dtype)
    totals = [jnp.stack(part) for part in parts]
    states = [jnp.stack(jax.tree.map(fill, part, identity)) for part in parts]
    join = lambda a, b: jnp.stack(combine((a[0], a[1]), (b[0], b[1])))
    distance = 1
    while distance < count:
        for n, back in enumerate(reverse):
            state, total = states[n], totals[n]
            for step in range(1, radix):
                reach = step * distance
                if reach >= count:
                    break
                got = passed_along(totals[n], axis, -reach if back else reach)
                valid = ranks[n] >= reach
                state = jnp.where(valid, join(got, state), state)
                if radix * distance < count:
                    total = jnp.where(valid, join(got, total), total)
            states[n], totals[n] = state, total
        distance *= radix
    return [(s[0], s[1]) for s in states]


def summed(part, axis):
    count = lax.axis_size(axis)
    if count & (count - 1):
        return lax.psum(part, axis)
    distance = 1
    while distance < count:
        part = part + lax.ppermute(part, axis, [(i, i ^ distance) for i in range(count)])
        distance *= 2
    return part


def conv_silu(extended, weights, row_count):
    summed = weights[0] * extended[0:row_count]
    for offset in range(1, CONV):
        summed = summed + weights[offset] * extended[offset : offset + row_count]
    return jax.nn.silu(summed)


def normed(entries):
    return entries * lax.rsqrt(jnp.sum(entries * entries, axis=-1, keepdims=True) + 1e-06)


def wy_factors(key_rows, value_rows, rates):
    weighted = key_rows * rates[:, None]
    strict = jnp.tril(jnp.dot(weighted, key_rows.T, precision=HIGHEST), -1)
    system = jnp.eye(strict.shape[0], dtype=strict.dtype) + strict
    w_keys = jax.scipy.linalg.solve_triangular(system, weighted, lower=True, unit_diagonal=True)
    w_values = jax.scipy.linalg.solve_triangular(
        system, value_rows * rates[:, None], lower=True, unit_diagonal=True
    )
    return (w_keys, w_values)


def block_step(state, block):
    query_rows, key_rows, value_rows, rates = block
    w_keys, w_values = wy_factors(key_rows, value_rows, rates)
    fresh = w_values - jnp.dot(w_keys, state, precision=HIGHEST)
    scores = jnp.tril(jnp.dot(query_rows, key_rows.T, precision=HIGHEST))
    output = jnp.dot(query_rows, state, precision=HIGHEST) + jnp.dot(
        scores, fresh, precision=HIGHEST
    )
    return (state + jnp.dot(key_rows.T, fresh, precision=HIGHEST), output)


def local_forward(ext_q, ext_k, ext_v, conv_three, logits, start_state):
    row_count = logits.shape[0]
    queries = normed(conv_silu(ext_q, conv_three[0], row_count))
    key_act = normed(conv_silu(ext_k, conv_three[1], row_count))
    value_act = conv_silu(ext_v, conv_three[2], row_count)
    rates = jax.nn.sigmoid(logits)
    blocks = row_count // BLOCK
    shaped = (
        queries.reshape(blocks, BLOCK, FEATURE_DIM),
        key_act.reshape(blocks, BLOCK, FEATURE_DIM),
        value_act.reshape(blocks, BLOCK, FEATURE_DIM),
        rates.reshape(blocks, BLOCK),
    )
    final, outputs = lax.scan(block_step, start_state, shaped)
    return (outputs.reshape(row_count, FEATURE_DIM), final)


def transition(ext_k, ext_v, conv_three, logits):
    row_count = logits.shape[0]
    key_act = normed(conv_silu(ext_k, conv_three[1], row_count))
    value_act = conv_silu(ext_v, conv_three[2], row_count)
    rates = jax.nn.sigmoid(logits)
    blocks = row_count // BLOCK
    shaped = (
        key_act.reshape(blocks, BLOCK, FEATURE_DIM),
        value_act.reshape(blocks, BLOCK, FEATURE_DIM),
        rates.reshape(blocks, BLOCK),
    )
    identity = jnp.eye(FEATURE_DIM, dtype=jnp.float32)

    def advance(carry, block):
        key_rows, value_rows, block_rates = block
        w_keys, w_values = wy_factors(key_rows, value_rows, block_rates)
        decay = identity - jnp.dot(key_rows.T, w_keys, precision=HIGHEST)
        written = jnp.dot(key_rows.T, w_values, precision=HIGHEST)
        return (
            (
                jnp.dot(decay, carry[0], precision=HIGHEST),
                jnp.dot(decay, carry[1], precision=HIGHEST) + written,
            ),
            None,
        )

    pairs, _ = lax.scan(
        advance, (identity, jnp.zeros((FEATURE_DIM, FEATURE_DIM), jnp.float32)), shaped
    )
    return pairs


def combine_pairs(earlier, later):
    product = jnp.matmul(later[0], earlier[0], precision=HIGHEST)
    offset_term = jnp.matmul(later[0], earlier[1], precision=HIGHEST) + later[1]
    return (product, offset_term)


def on_device(q_raw, k_raw, v_raw, conv_weight, beta_logit, out_weight, out_grad):
    row_count = q_raw.shape[0]
    col_count = q_raw.shape[1]
    head_count = col_count // FEATURE_DIM
    margin = CONV - 1
    tail = row_count - margin
    rim_rows = passed_along((q_raw[tail:], k_raw[tail:], v_raw[tail:]), "ctx", 1)

    def extend(rim_part, main_part):
        joined = jnp.concatenate([rim_part, main_part], 0).astype(jnp.float32)
        return joined.reshape(margin + row_count, head_count, FEATURE_DIM).transpose(1, 0, 2)

    ext_q = extend(rim_rows[0], q_raw)
    ext_k = extend(rim_rows[1], k_raw)
    ext_v = extend(rim_rows[2], v_raw)
    conv_heads = conv_weight.reshape(3, CONV, head_count, FEATURE_DIM).transpose(2, 0, 1, 3)
    out_cot = lax.dot_general(
        lax.all_gather(out_grad, "head", axis=1, tiled=True),
        out_weight,
        (((1,), (1,)), ((), ())),
        preferred_element_type=jnp.float32,
    )
    out_cot = out_cot.reshape(row_count, head_count, FEATURE_DIM).transpose(1, 0, 2)
    pairs = jax.vmap(transition)(ext_k, ext_v, conv_heads, beta_logit)
    identity = jnp.broadcast_to(
        jnp.eye(FEATURE_DIM, dtype=jnp.float32), (head_count, FEATURE_DIM, FEATURE_DIM)
    )
    zero_state = jnp.zeros((head_count, FEATURE_DIM, FEATURE_DIM), jnp.float32)
    batched = jax.vmap(local_forward)
    adjoint_map = jnp.swapaxes(pairs[0], 1, 2)
    _, seed_backward = jax.vjp(batched, ext_q, ext_k, ext_v, conv_heads, beta_logit, zero_state)
    local_seed = seed_backward((out_cot, zero_state))[5]
    carried, suffix = carried_in(
        [pairs, (adjoint_map, local_seed)],
        "ctx",
        combine_pairs,
        (identity, zero_state),
        [False, True],
    )
    start_state = carried[1]
    _, backward = jax.vjp(batched, ext_q, ext_k, ext_v, conv_heads, beta_logit, start_state)
    grads = backward((out_cot, suffix[1]))
    rim_back = passed_along(
        (grads[0][:, :margin], grads[1][:, :margin], grads[2][:, :margin]), "ctx", -1
    )

    def finish(grad_ext, rim_part):
        main_part = grad_ext[:, margin:]
        main_part = jnp.concatenate([main_part[:, :tail], main_part[:, tail:] + rim_part], 1)
        return main_part.transpose(1, 0, 2).reshape(row_count, col_count)

    conv_local = grads[3].transpose(1, 2, 0, 3).reshape(3, CONV, col_count)
    scale = 1.0 / math.sqrt(row_count * lax.axis_size("ctx"))
    conv_total = summed(conv_local, "ctx") * scale
    return (
        finish(grads[0], rim_back[0]),
        finish(grads[1], rim_back[1]),
        finish(grads[2], rim_back[2]),
        conv_total,
        grads[4],
    )


def solution(mesh):
    return jax.shard_map(
        on_device,
        mesh=mesh,
        in_specs=(
            P("ctx", "head"),
            P("ctx", "head"),
            P("ctx", "head"),
            P(None, None, "head"),
            P("head", "ctx"),
            P("head", None),
            P("ctx", "head"),
        ),
        out_specs=(
            P("ctx", "head"),
            P("ctx", "head"),
            P("ctx", "head"),
            P(None, None, "head"),
            P("head", "ctx"),
        ),
        check_vma=False,
    )
```

```python
import math

import jax
import jax.numpy as jnp
from jax import lax
from jax.sharding import PartitionSpec as P

FEATURE_DIM = 128
CONV = 4
BLOCK = 64


HIGHEST = lax.Precision.HIGHEST


def passed_along(block, axis, distance):
    devices = range(lax.axis_size(axis))
    route = [(i - distance, i) for i in devices if i - distance in devices]
    return lax.ppermute(block, axis, route)


def carried_in(parts, axis, combine, identity, reverse, radix=4):
    count = lax.axis_size(axis)
    place = lax.axis_index(axis)
    ranks = [count - 1 - place if back else place for back in reverse]
    fill = lambda a, e: jnp.zeros_like(a) + jnp.asarray(e, a.dtype)
    totals = [jnp.stack(part) for part in parts]
    states = [jnp.stack(jax.tree.map(fill, part, identity)) for part in parts]
    join = lambda a, b: jnp.stack(combine((a[0], a[1]), (b[0], b[1])))
    distance = 1
    while distance < count:
        for n, back in enumerate(reverse):
            state, total = states[n], totals[n]
            for step in range(1, radix):
                reach = step * distance
                if reach >= count:
                    break
                got = passed_along(totals[n], axis, -reach if back else reach)
                valid = ranks[n] >= reach
                state = jnp.where(valid, join(got, state), state)
                if radix * distance < count:
                    total = jnp.where(valid, join(got, total), total)
            states[n], totals[n] = state, total
        distance *= radix
    return [(s[0], s[1]) for s in states]


def summed(part, axis):
    count = lax.axis_size(axis)
    place = lax.axis_index(axis)
    distance = 1
    while distance < count:
        radix = 4 if (count // distance) % 4 == 0 else 2
        if (count // distance) % radix:
            return lax.psum(part, axis)
        digit = (place // distance) % radix
        got = [part]
        for shift in range(1, radix):
            route = []
            for i in range(count):
                own = (i // distance) % radix
                route.append((i + ((own + shift) % radix - own) * distance, i))
            got.append(lax.ppermute(part, axis, route))
        ordered = jnp.stack(got)[(jnp.arange(radix) - digit) % radix]
        if radix == 4:
            part = (ordered[0] + ordered[1]) + (ordered[2] + ordered[3])
        else:
            part = ordered[0] + ordered[1]
        distance *= radix
    return part


def conv_silu(extended, weights, row_count):
    summed = weights[0] * extended[0:row_count]
    for offset in range(1, CONV):
        summed = summed + weights[offset] * extended[offset : offset + row_count]
    return jax.nn.silu(summed)


def normed(entries):
    return entries * lax.rsqrt(jnp.sum(entries * entries, axis=-1, keepdims=True) + 1e-06)


def wy_factors(key_rows, value_rows, rates):
    weighted = key_rows * rates[:, None]
    strict = jnp.tril(jnp.dot(weighted, key_rows.T, precision=HIGHEST), -1)
    system = jnp.eye(strict.shape[0], dtype=strict.dtype) + strict
    w_keys = jax.scipy.linalg.solve_triangular(system, weighted, lower=True, unit_diagonal=True)
    w_values = jax.scipy.linalg.solve_triangular(
        system, value_rows * rates[:, None], lower=True, unit_diagonal=True
    )
    return (w_keys, w_values)


def block_step(state, block):
    query_rows, key_rows, w_keys, w_values, scores = block
    fresh = w_values - jnp.dot(w_keys, state, precision=HIGHEST)
    output = jnp.dot(query_rows, state, precision=HIGHEST) + jnp.dot(
        scores, fresh, precision=HIGHEST
    )
    return (state + jnp.dot(key_rows.T, fresh, precision=HIGHEST), output)


def prepare(ext_q, ext_k, ext_v, conv_three, logits):
    row_count = logits.shape[0]
    blocks = row_count // BLOCK
    shape = (blocks, BLOCK, FEATURE_DIM)
    queries = normed(conv_silu(ext_q, conv_three[0], row_count)).reshape(shape)
    key_act = normed(conv_silu(ext_k, conv_three[1], row_count)).reshape(shape)
    value_act = conv_silu(ext_v, conv_three[2], row_count).reshape(shape)
    rates = jax.nn.sigmoid(logits).reshape(blocks, BLOCK)
    w_keys, w_values = jax.vmap(wy_factors)(key_act, value_act, rates)
    scores = jnp.tril(jnp.einsum("bif,bjf->bij", queries, key_act, precision=HIGHEST))
    return (queries, key_act, w_keys, w_values, scores)


def recur(prepared, start_state):
    final, outputs = lax.scan(block_step, start_state, prepared, unroll=True)
    return (outputs.reshape(-1, FEATURE_DIM), final)


def transition(prepared):
    _, key_act, w_keys, w_values, _ = prepared
    identity = jnp.eye(FEATURE_DIM, dtype=jnp.float32)
    decay = identity - jnp.einsum("bif,big->bfg", key_act, w_keys, precision=HIGHEST)
    written = jnp.einsum("bif,big->bfg", key_act, w_values, precision=HIGHEST)
    pair = (decay[0], written[0])
    for block in range(1, decay.shape[0]):
        pair = (
            jnp.dot(decay[block], pair[0], precision=HIGHEST),
            jnp.dot(decay[block], pair[1], precision=HIGHEST) + written[block],
        )
    return pair


def combine_pairs(earlier, later):
    product = jnp.matmul(later[0], earlier[0], precision=HIGHEST)
    offset_term = jnp.matmul(later[0], earlier[1], precision=HIGHEST) + later[1]
    return (product, offset_term)


def on_device(q_raw, k_raw, v_raw, conv_weight, beta_logit, out_weight, out_grad):
    row_count = q_raw.shape[0]
    col_count = q_raw.shape[1]
    head_count = col_count // FEATURE_DIM
    margin = CONV - 1
    tail = row_count - margin
    rim_rows = passed_along((q_raw[tail:], k_raw[tail:], v_raw[tail:]), "ctx", 1)

    def extend(rim_part, main_part):
        joined = jnp.concatenate([rim_part, main_part], 0).astype(jnp.float32)
        return joined.reshape(margin + row_count, head_count, FEATURE_DIM).transpose(1, 0, 2)

    ext_q = extend(rim_rows[0], q_raw)
    ext_k = extend(rim_rows[1], k_raw)
    ext_v = extend(rim_rows[2], v_raw)
    conv_heads = conv_weight.reshape(3, CONV, head_count, FEATURE_DIM).transpose(2, 0, 1, 3)
    out_cot = lax.dot_general(
        lax.all_gather(out_grad, "head", axis=1, tiled=True),
        out_weight,
        (((1,), (1,)), ((), ())),
        preferred_element_type=jnp.float32,
    )
    out_cot = out_cot.reshape(row_count, head_count, FEATURE_DIM).transpose(1, 0, 2)
    prepared, prepare_back = jax.vjp(
        jax.vmap(prepare), ext_q, ext_k, ext_v, conv_heads, beta_logit
    )
    pairs = jax.vmap(transition)(prepared)
    identity = jnp.broadcast_to(
        jnp.eye(FEATURE_DIM, dtype=jnp.float32), (head_count, FEATURE_DIM, FEATURE_DIM)
    )
    zero_state = jnp.zeros((head_count, FEATURE_DIM, FEATURE_DIM), jnp.float32)
    batched = jax.vmap(recur)
    adjoint_map = jnp.swapaxes(pairs[0], 1, 2)
    _, seed_backward = jax.vjp(lambda state: batched(prepared, state), zero_state)
    local_seed = seed_backward((out_cot, zero_state))[0]
    carried, suffix = carried_in(
        [pairs, (adjoint_map, local_seed)],
        "ctx",
        combine_pairs,
        (identity, zero_state),
        [False, True],
    )
    _, backward = jax.vjp(batched, prepared, carried[1])
    grads = prepare_back(backward((out_cot, suffix[1]))[0])
    rim_back = passed_along(
        (grads[0][:, :margin], grads[1][:, :margin], grads[2][:, :margin]), "ctx", -1
    )

    def finish(grad_ext, rim_part):
        main_part = grad_ext[:, margin:]
        main_part = jnp.concatenate([main_part[:, :tail], main_part[:, tail:] + rim_part], 1)
        return main_part.transpose(1, 0, 2).reshape(row_count, col_count)

    conv_local = grads[3].transpose(1, 2, 0, 3).reshape(3, CONV, col_count)
    scale = 1.0 / math.sqrt(row_count * lax.axis_size("ctx"))
    conv_total = summed(conv_local, "ctx") * scale
    return (
        finish(grads[0], rim_back[0]),
        finish(grads[1], rim_back[1]),
        finish(grads[2], rim_back[2]),
        conv_total,
        grads[4],
    )


def solution(mesh):
    return jax.shard_map(
        on_device,
        mesh=mesh,
        in_specs=(
            P("ctx", "head"),
            P("ctx", "head"),
            P("ctx", "head"),
            P(None, None, "head"),
            P("head", "ctx"),
            P("head", None),
            P("ctx", "head"),
        ),
        out_specs=(
            P("ctx", "head"),
            P("ctx", "head"),
            P("ctx", "head"),
            P(None, None, "head"),
            P("head", "ctx"),
        ),
        check_vma=False,
    )
```

```python
import math

import jax
import jax.numpy as jnp
from jax import lax
from jax.sharding import PartitionSpec as P

FEATURE_DIM = 128
CONV = 4
BLOCK = 64


HIGHEST = lax.Precision.HIGHEST


def passed_along(block, axis, distance):
    devices = range(lax.axis_size(axis))
    route = [(i - distance, i) for i in devices if i - distance in devices]
    return lax.ppermute(block, axis, route)


def carried_in(parts, axis, combine, identity, reverse, radix=2):
    count = lax.axis_size(axis)
    place = lax.axis_index(axis)
    ranks = [count - 1 - place if back else place for back in reverse]
    fill = lambda a, e: jnp.zeros_like(a) + jnp.asarray(e, a.dtype)
    totals = [jnp.stack(part) for part in parts]
    states = [jnp.stack(jax.tree.map(fill, part, identity)) for part in parts]
    join = lambda a, b: jnp.stack(combine((a[0], a[1]), (b[0], b[1])))
    distance = 1
    while distance < count:
        for n, back in enumerate(reverse):
            state, total = states[n], totals[n]
            for step in range(1, radix):
                reach = step * distance
                if reach >= count:
                    break
                got = passed_along(totals[n], axis, -reach if back else reach)
                valid = ranks[n] >= reach
                state = jnp.where(valid, join(got, state), state)
                if radix * distance < count:
                    total = jnp.where(valid, join(got, total), total)
            states[n], totals[n] = state, total
        distance *= radix
    return [(s[0], s[1]) for s in states]


def summed(part, axis):
    return jnp.sum(lax.all_gather(part, axis), axis=0)


def conv_silu(extended, weights, row_count):
    summed = weights[0] * extended[0:row_count]
    for offset in range(1, CONV):
        summed = summed + weights[offset] * extended[offset : offset + row_count]
    return jax.nn.silu(summed)


def normed(entries):
    return entries * lax.rsqrt(jnp.sum(entries * entries, axis=-1, keepdims=True) + 1e-06)


def wy_factors(key_rows, value_rows, rates):
    weighted = key_rows * rates[:, None]
    strict = jnp.tril(jnp.dot(weighted, key_rows.T, precision=HIGHEST), -1)
    system = jnp.eye(strict.shape[0], dtype=strict.dtype) + strict
    w_keys = jax.scipy.linalg.solve_triangular(system, weighted, lower=True, unit_diagonal=True)
    w_values = jax.scipy.linalg.solve_triangular(
        system, value_rows * rates[:, None], lower=True, unit_diagonal=True
    )
    return (w_keys, w_values)


def block_step(state, block):
    query_rows, key_rows, w_keys, w_values, scores = block
    fresh = w_values - jnp.dot(w_keys, state, precision=HIGHEST)
    output = jnp.dot(query_rows, state, precision=HIGHEST) + jnp.dot(
        scores, fresh, precision=HIGHEST
    )
    return (state + jnp.dot(key_rows.T, fresh, precision=HIGHEST), output)


def prepare(ext_q, ext_k, ext_v, conv_three, logits):
    row_count = logits.shape[0]
    blocks = row_count // BLOCK
    shape = (blocks, BLOCK, FEATURE_DIM)
    queries = normed(conv_silu(ext_q, conv_three[0], row_count)).reshape(shape)
    key_act = normed(conv_silu(ext_k, conv_three[1], row_count)).reshape(shape)
    value_act = conv_silu(ext_v, conv_three[2], row_count).reshape(shape)
    rates = jax.nn.sigmoid(logits).reshape(blocks, BLOCK)
    w_keys, w_values = jax.vmap(wy_factors)(key_act, value_act, rates)
    scores = jnp.tril(jnp.einsum("bif,bjf->bij", queries, key_act, precision=HIGHEST))
    return (queries, key_act, w_keys, w_values, scores)


def recur(prepared, start_state):
    final, outputs = lax.scan(block_step, start_state, prepared, unroll=True)
    return (outputs.reshape(-1, FEATURE_DIM), final)


def transition(prepared):
    _, key_act, w_keys, w_values, _ = prepared
    identity = jnp.eye(FEATURE_DIM, dtype=jnp.float32)
    decay = identity - jnp.einsum("bif,big->bfg", key_act, w_keys, precision=HIGHEST)
    written = jnp.einsum("bif,big->bfg", key_act, w_values, precision=HIGHEST)
    pair = (decay[0], written[0])
    for block in range(1, decay.shape[0]):
        pair = (
            jnp.dot(decay[block], pair[0], precision=HIGHEST),
            jnp.dot(decay[block], pair[1], precision=HIGHEST) + written[block],
        )
    return pair


def combine_pairs(earlier, later):
    product = jnp.matmul(later[0], earlier[0], precision=HIGHEST)
    offset_term = jnp.matmul(later[0], earlier[1], precision=HIGHEST) + later[1]
    return (product, offset_term)


def on_device(q_raw, k_raw, v_raw, conv_weight, beta_logit, out_weight, out_grad):
    row_count = q_raw.shape[0]
    col_count = q_raw.shape[1]
    head_count = col_count // FEATURE_DIM
    margin = CONV - 1
    tail = row_count - margin
    rim_rows = passed_along(jnp.stack([q_raw[tail:], k_raw[tail:], v_raw[tail:]]), "ctx", 1)

    def extend(rim_part, main_part):
        joined = jnp.concatenate([rim_part, main_part], 0).astype(jnp.float32)
        return joined.reshape(margin + row_count, head_count, FEATURE_DIM).transpose(1, 0, 2)

    ext_q = extend(rim_rows[0], q_raw)
    ext_k = extend(rim_rows[1], k_raw)
    ext_v = extend(rim_rows[2], v_raw)
    conv_heads = conv_weight.reshape(3, CONV, head_count, FEATURE_DIM).transpose(2, 0, 1, 3)
    out_cot = lax.dot_general(
        lax.all_gather(out_grad, "head", axis=1, tiled=True),
        out_weight,
        (((1,), (1,)), ((), ())),
        preferred_element_type=jnp.float32,
    )
    out_cot = out_cot.reshape(row_count, head_count, FEATURE_DIM).transpose(1, 0, 2)
    prepared, prepare_back = jax.vjp(
        jax.vmap(prepare), ext_q, ext_k, ext_v, conv_heads, beta_logit
    )
    pairs = jax.vmap(transition)(prepared)
    identity = jnp.broadcast_to(
        jnp.eye(FEATURE_DIM, dtype=jnp.float32), (head_count, FEATURE_DIM, FEATURE_DIM)
    )
    zero_state = jnp.zeros((head_count, FEATURE_DIM, FEATURE_DIM), jnp.float32)
    batched = jax.vmap(recur)
    adjoint_map = jnp.swapaxes(pairs[0], 1, 2)
    _, seed_backward = jax.vjp(lambda state: batched(prepared, state), zero_state)
    local_seed = seed_backward((out_cot, zero_state))[0]
    carried, suffix = carried_in(
        [pairs, (adjoint_map, local_seed)],
        "ctx",
        combine_pairs,
        (identity, zero_state),
        [False, True],
    )
    _, backward = jax.vjp(batched, prepared, carried[1])
    grads = prepare_back(backward((out_cot, suffix[1]))[0])
    rim_back = passed_along(
        jnp.stack([grads[0][:, :margin], grads[1][:, :margin], grads[2][:, :margin]]), "ctx", -1
    )

    def finish(grad_ext, rim_part):
        main_part = grad_ext[:, margin:]
        main_part = jnp.concatenate([main_part[:, :tail], main_part[:, tail:] + rim_part], 1)
        return main_part.transpose(1, 0, 2).reshape(row_count, col_count)

    conv_local = grads[3].transpose(1, 2, 0, 3).reshape(3, CONV, col_count)
    scale = 1.0 / math.sqrt(row_count * lax.axis_size("ctx"))
    conv_total = summed(conv_local, "ctx") * scale
    return (
        finish(grads[0], rim_back[0]),
        finish(grads[1], rim_back[1]),
        finish(grads[2], rim_back[2]),
        conv_total,
        grads[4],
    )


def solution(mesh):
    return jax.shard_map(
        on_device,
        mesh=mesh,
        in_specs=(
            P("ctx", "head"),
            P("ctx", "head"),
            P("ctx", "head"),
            P(None, None, "head"),
            P("head", "ctx"),
            P("head", None),
            P("ctx", "head"),
        ),
        out_specs=(
            P("ctx", "head"),
            P("ctx", "head"),
            P("ctx", "head"),
            P(None, None, "head"),
            P("head", "ctx"),
        ),
        check_vma=False,
    )
```

```python
import math

import jax
import jax.numpy as jnp
from jax import lax
from jax.sharding import PartitionSpec as P

FEATURE_DIM = 128
CONV = 4
BLOCK = 64


HIGHEST = lax.Precision.HIGHEST


def passed_along(block, axis, distance):
    devices = range(lax.axis_size(axis))
    route = [(i - distance, i) for i in devices if i - distance in devices]
    return lax.ppermute(block, axis, route)


def carried_in(parts, axis, combine, identity, reverse, radix=4):
    count = lax.axis_size(axis)
    place = lax.axis_index(axis)
    ranks = [count - 1 - place if back else place for back in reverse]
    fill = lambda a, e: jnp.zeros_like(a) + jnp.asarray(e, a.dtype)
    totals = [jnp.stack(part) for part in parts]
    states = [jnp.stack(jax.tree.map(fill, part, identity)) for part in parts]
    join = lambda a, b: jnp.stack(combine((a[0], a[1]), (b[0], b[1])))
    distance = 1
    while distance < count:
        for n, back in enumerate(reverse):
            state, total = states[n], totals[n]
            for step in range(1, radix):
                reach = step * distance
                if reach >= count:
                    break
                got = passed_along(totals[n], axis, -reach if back else reach)
                valid = ranks[n] >= reach
                state = jnp.where(valid, join(got, state), state)
                if radix * distance < count:
                    total = jnp.where(valid, join(got, total), total)
            states[n], totals[n] = state, total
        distance *= radix
    return [(s[0], s[1]) for s in states]


def summed(part, axis):
    count = lax.axis_size(axis)
    place = lax.axis_index(axis)
    distance = 1
    while distance < count:
        radix = 4 if (count // distance) % 4 == 0 else 2
        if (count // distance) % radix:
            return lax.psum(part, axis)
        digit = (place // distance) % radix
        got = [part]
        for shift in range(1, radix):
            route = []
            for i in range(count):
                own = (i // distance) % radix
                route.append((i + ((own + shift) % radix - own) * distance, i))
            got.append(lax.ppermute(part, axis, route))
        ordered = jnp.stack(got)[(jnp.arange(radix) - digit) % radix]
        if radix == 4:
            part = (ordered[0] + ordered[1]) + (ordered[2] + ordered[3])
        else:
            part = ordered[0] + ordered[1]
        distance *= radix
    return part


def conv_silu(extended, weights, row_count):
    summed = weights[0] * extended[0:row_count]
    for offset in range(1, CONV):
        summed = summed + weights[offset] * extended[offset : offset + row_count]
    return jax.nn.silu(summed)


def normed(entries):
    return entries * lax.rsqrt(jnp.sum(entries * entries, axis=-1, keepdims=True) + 1e-06)


def wy_factors(key_rows, value_rows, rates):
    weighted = key_rows * rates[:, None]
    strict = jnp.tril(jnp.dot(weighted, key_rows.T, precision=HIGHEST), -1)
    system = jnp.eye(strict.shape[0], dtype=strict.dtype) + strict
    w_keys = jax.scipy.linalg.solve_triangular(system, weighted, lower=True, unit_diagonal=True)
    w_values = jax.scipy.linalg.solve_triangular(
        system, value_rows * rates[:, None], lower=True, unit_diagonal=True
    )
    return (w_keys, w_values)


def block_step(state, block):
    query_rows, key_rows, w_keys, w_values, scores = block
    fresh = w_values - jnp.dot(w_keys, state, precision=HIGHEST)
    output = jnp.dot(query_rows, state, precision=HIGHEST) + jnp.dot(
        scores, fresh, precision=HIGHEST
    )
    return (state + jnp.dot(key_rows.T, fresh, precision=HIGHEST), output)


def prepare(ext_q, ext_k, ext_v, conv_three, logits):
    row_count = logits.shape[0]
    blocks = row_count // BLOCK
    shape = (blocks, BLOCK, FEATURE_DIM)
    queries = normed(conv_silu(ext_q, conv_three[0], row_count)).reshape(shape)
    key_act = normed(conv_silu(ext_k, conv_three[1], row_count)).reshape(shape)
    value_act = conv_silu(ext_v, conv_three[2], row_count).reshape(shape)
    rates = jax.nn.sigmoid(logits).reshape(blocks, BLOCK)
    w_keys, w_values = jax.vmap(wy_factors)(key_act, value_act, rates)
    scores = jnp.tril(jnp.einsum("bif,bjf->bij", queries, key_act, precision=HIGHEST))
    return (queries, key_act, w_keys, w_values, scores)


def recur(prepared, start_state):
    final, outputs = lax.scan(block_step, start_state, prepared, unroll=True)
    return (outputs.reshape(-1, FEATURE_DIM), final)


def transition(prepared):
    _, key_act, w_keys, w_values, _ = prepared
    identity = jnp.eye(FEATURE_DIM, dtype=jnp.float32)
    decay = identity - jnp.einsum("bif,big->bfg", key_act, w_keys, precision=HIGHEST)
    written = jnp.einsum("bif,big->bfg", key_act, w_values, precision=HIGHEST)
    pair = (decay[0], written[0])
    for block in range(1, decay.shape[0]):
        pair = (
            jnp.dot(decay[block], pair[0], precision=HIGHEST),
            jnp.dot(decay[block], pair[1], precision=HIGHEST) + written[block],
        )
    return pair


def combine_pairs(earlier, later):
    product = jnp.matmul(later[0], earlier[0], precision=HIGHEST)
    offset_term = jnp.matmul(later[0], earlier[1], precision=HIGHEST) + later[1]
    return (product, offset_term)


def on_device(q_raw, k_raw, v_raw, conv_weight, beta_logit, out_weight, out_grad):
    row_count = q_raw.shape[0]
    col_count = q_raw.shape[1]
    head_count = col_count // FEATURE_DIM
    margin = CONV - 1
    tail = row_count - margin
    rim_rows = passed_along(jnp.stack([q_raw[tail:], k_raw[tail:], v_raw[tail:]]), "ctx", 1)

    def extend(rim_part, main_part):
        joined = jnp.concatenate([rim_part, main_part], 0).astype(jnp.float32)
        return joined.reshape(margin + row_count, head_count, FEATURE_DIM).transpose(1, 0, 2)

    ext_q = extend(rim_rows[0], q_raw)
    ext_k = extend(rim_rows[1], k_raw)
    ext_v = extend(rim_rows[2], v_raw)
    conv_heads = conv_weight.reshape(3, CONV, head_count, FEATURE_DIM).transpose(2, 0, 1, 3)
    out_cot = lax.dot_general(
        lax.all_gather(out_grad, "head", axis=1, tiled=True),
        out_weight,
        (((1,), (1,)), ((), ())),
        preferred_element_type=jnp.float32,
    )
    out_cot = out_cot.reshape(row_count, head_count, FEATURE_DIM).transpose(1, 0, 2)
    prepared, prepare_back = jax.vjp(
        jax.vmap(prepare), ext_q, ext_k, ext_v, conv_heads, beta_logit
    )
    pairs = jax.vmap(transition)(prepared)
    identity = jnp.broadcast_to(
        jnp.eye(FEATURE_DIM, dtype=jnp.float32), (head_count, FEATURE_DIM, FEATURE_DIM)
    )
    zero_state = jnp.zeros((head_count, FEATURE_DIM, FEATURE_DIM), jnp.float32)
    batched = jax.vmap(recur)
    adjoint_map = jnp.swapaxes(pairs[0], 1, 2)
    _, seed_backward = jax.vjp(lambda state: batched(prepared, state), zero_state)
    local_seed = seed_backward((out_cot, zero_state))[0]
    carried, suffix = carried_in(
        [pairs, (adjoint_map, local_seed)],
        "ctx",
        combine_pairs,
        (identity, zero_state),
        [False, True],
    )
    _, backward = jax.vjp(batched, prepared, carried[1])
    grads = prepare_back(backward((out_cot, suffix[1]))[0])
    rim_back = passed_along(
        jnp.stack([grads[0][:, :margin], grads[1][:, :margin], grads[2][:, :margin]]), "ctx", -1
    )

    def finish(grad_ext, rim_part):
        main_part = grad_ext[:, margin:]
        main_part = jnp.concatenate([main_part[:, :tail], main_part[:, tail:] + rim_part], 1)
        return main_part.transpose(1, 0, 2).reshape(row_count, col_count)

    conv_local = grads[3].transpose(1, 2, 0, 3).reshape(3, CONV, col_count)
    scale = 1.0 / math.sqrt(row_count * lax.axis_size("ctx"))
    conv_total = summed(conv_local, "ctx") * scale
    return (
        finish(grads[0], rim_back[0]),
        finish(grads[1], rim_back[1]),
        finish(grads[2], rim_back[2]),
        conv_total,
        grads[4],
    )


def solution(mesh):
    return jax.shard_map(
        on_device,
        mesh=mesh,
        in_specs=(
            P("ctx", "head"),
            P("ctx", "head"),
            P("ctx", "head"),
            P(None, None, "head"),
            P("head", "ctx"),
            P("head", None),
            P("ctx", "head"),
        ),
        out_specs=(
            P("ctx", "head"),
            P("ctx", "head"),
            P("ctx", "head"),
            P(None, None, "head"),
            P("head", "ctx"),
        ),
        check_vma=False,
    )
```

```python
import math

import jax
import jax.numpy as jnp
from jax import lax
from jax.sharding import PartitionSpec as P

FEATURE_DIM = 128
CONV = 4
BLOCK = 64


HIGHEST = lax.Precision.HIGHEST


def passed_along(block, axis, distance):
    devices = range(lax.axis_size(axis))
    route = [(i - distance, i) for i in devices if i - distance in devices]
    return lax.ppermute(block, axis, route)


def carried_in(parts, axis, combine, identity, reverse, radix=4):
    count = lax.axis_size(axis)
    place = lax.axis_index(axis)
    ranks = [count - 1 - place if back else place for back in reverse]
    fill = lambda a, e: jnp.zeros_like(a) + jnp.asarray(e, a.dtype)
    totals = [jnp.stack(part) for part in parts]
    states = [jnp.stack(jax.tree.map(fill, part, identity)) for part in parts]
    join = lambda a, b: jnp.stack(combine((a[0], a[1]), (b[0], b[1])))
    distance = 1
    while distance < count:
        for n, back in enumerate(reverse):
            state, total = states[n], totals[n]
            for step in range(1, radix):
                reach = step * distance
                if reach >= count:
                    break
                got = passed_along(totals[n], axis, -reach if back else reach)
                valid = ranks[n] >= reach
                state = jnp.where(valid, join(got, state), state)
                if radix * distance < count:
                    total = jnp.where(valid, join(got, total), total)
            states[n], totals[n] = state, total
        distance *= radix
    return [(s[0], s[1]) for s in states]


def summed(part, axis):
    count = lax.axis_size(axis)
    place = lax.axis_index(axis)
    distance = 1
    while distance < count:
        radix = 2
        if (count // distance) % radix:
            return lax.psum(part, axis)
        digit = (place // distance) % radix
        got = [part]
        for shift in range(1, radix):
            route = []
            for i in range(count):
                own = (i // distance) % radix
                route.append((i + ((own + shift) % radix - own) * distance, i))
            got.append(lax.ppermute(part, axis, route))
        ordered = jnp.stack(got)[(jnp.arange(radix) - digit) % radix]
        if radix == 4:
            part = (ordered[0] + ordered[1]) + (ordered[2] + ordered[3])
        else:
            part = ordered[0] + ordered[1]
        distance *= radix
    return part


def conv_silu(extended, weights, row_count):
    summed = weights[0] * extended[0:row_count]
    for offset in range(1, CONV):
        summed = summed + weights[offset] * extended[offset : offset + row_count]
    return jax.nn.silu(summed)


def normed(entries):
    return entries * lax.rsqrt(jnp.sum(entries * entries, axis=-1, keepdims=True) + 1e-06)


def wy_factors(key_rows, value_rows, rates):
    weighted = key_rows * rates[:, None]
    strict = jnp.tril(jnp.dot(weighted, key_rows.T, precision=HIGHEST), -1)
    system = jnp.eye(strict.shape[0], dtype=strict.dtype) + strict
    w_keys = jax.scipy.linalg.solve_triangular(system, weighted, lower=True, unit_diagonal=True)
    w_values = jax.scipy.linalg.solve_triangular(
        system, value_rows * rates[:, None], lower=True, unit_diagonal=True
    )
    return (w_keys, w_values)


def block_step(state, block):
    query_rows, key_rows, w_keys, w_values, scores = block
    fresh = w_values - jnp.dot(w_keys, state, precision=HIGHEST)
    output = jnp.dot(query_rows, state, precision=HIGHEST) + jnp.dot(
        scores, fresh, precision=HIGHEST
    )
    return (state + jnp.dot(key_rows.T, fresh, precision=HIGHEST), output)


def prepare(ext_q, ext_k, ext_v, conv_three, logits):
    row_count = logits.shape[0]
    blocks = row_count // BLOCK
    shape = (blocks, BLOCK, FEATURE_DIM)
    queries = normed(conv_silu(ext_q, conv_three[0], row_count)).reshape(shape)
    key_act = normed(conv_silu(ext_k, conv_three[1], row_count)).reshape(shape)
    value_act = conv_silu(ext_v, conv_three[2], row_count).reshape(shape)
    rates = jax.nn.sigmoid(logits).reshape(blocks, BLOCK)
    w_keys, w_values = jax.vmap(wy_factors)(key_act, value_act, rates)
    scores = jnp.tril(jnp.einsum("bif,bjf->bij", queries, key_act, precision=HIGHEST))
    return (queries, key_act, w_keys, w_values, scores)


def recur(prepared, start_state):
    final, outputs = lax.scan(block_step, start_state, prepared, unroll=True)
    return (outputs.reshape(-1, FEATURE_DIM), final)


def transition(prepared):
    _, key_act, w_keys, w_values, _ = prepared
    identity = jnp.eye(FEATURE_DIM, dtype=jnp.float32)
    decay = identity - jnp.einsum("bif,big->bfg", key_act, w_keys, precision=HIGHEST)
    written = jnp.einsum("bif,big->bfg", key_act, w_values, precision=HIGHEST)
    pair = (decay[0], written[0])
    for block in range(1, decay.shape[0]):
        pair = (
            jnp.dot(decay[block], pair[0], precision=HIGHEST),
            jnp.dot(decay[block], pair[1], precision=HIGHEST) + written[block],
        )
    return pair


def combine_pairs(earlier, later):
    product = jnp.matmul(later[0], earlier[0], precision=HIGHEST)
    offset_term = jnp.matmul(later[0], earlier[1], precision=HIGHEST) + later[1]
    return (product, offset_term)


def on_device(q_raw, k_raw, v_raw, conv_weight, beta_logit, out_weight, out_grad):
    row_count = q_raw.shape[0]
    col_count = q_raw.shape[1]
    head_count = col_count // FEATURE_DIM
    margin = CONV - 1
    tail = row_count - margin
    rim_rows = passed_along(jnp.stack([q_raw[tail:], k_raw[tail:], v_raw[tail:]]), "ctx", 1)

    def extend(rim_part, main_part):
        joined = jnp.concatenate([rim_part, main_part], 0).astype(jnp.float32)
        return joined.reshape(margin + row_count, head_count, FEATURE_DIM).transpose(1, 0, 2)

    ext_q = extend(rim_rows[0], q_raw)
    ext_k = extend(rim_rows[1], k_raw)
    ext_v = extend(rim_rows[2], v_raw)
    conv_heads = conv_weight.reshape(3, CONV, head_count, FEATURE_DIM).transpose(2, 0, 1, 3)
    out_cot = lax.dot_general(
        lax.all_gather(out_grad, "head", axis=1, tiled=True),
        out_weight,
        (((1,), (1,)), ((), ())),
        preferred_element_type=jnp.float32,
    )
    out_cot = out_cot.reshape(row_count, head_count, FEATURE_DIM).transpose(1, 0, 2)
    prepared, prepare_back = jax.vjp(
        jax.vmap(prepare), ext_q, ext_k, ext_v, conv_heads, beta_logit
    )
    pairs = jax.vmap(transition)(prepared)
    identity = jnp.broadcast_to(
        jnp.eye(FEATURE_DIM, dtype=jnp.float32), (head_count, FEATURE_DIM, FEATURE_DIM)
    )
    zero_state = jnp.zeros((head_count, FEATURE_DIM, FEATURE_DIM), jnp.float32)
    batched = jax.vmap(recur)
    adjoint_map = jnp.swapaxes(pairs[0], 1, 2)
    _, seed_backward = jax.vjp(lambda state: batched(prepared, state), zero_state)
    local_seed = seed_backward((out_cot, zero_state))[0]
    carried, suffix = carried_in(
        [pairs, (adjoint_map, local_seed)],
        "ctx",
        combine_pairs,
        (identity, zero_state),
        [False, True],
    )
    _, backward = jax.vjp(batched, prepared, carried[1])
    grads = prepare_back(backward((out_cot, suffix[1]))[0])
    rim_back = passed_along(
        jnp.stack([grads[0][:, :margin], grads[1][:, :margin], grads[2][:, :margin]]), "ctx", -1
    )

    def finish(grad_ext, rim_part):
        main_part = grad_ext[:, margin:]
        main_part = jnp.concatenate([main_part[:, :tail], main_part[:, tail:] + rim_part], 1)
        return main_part.transpose(1, 0, 2).reshape(row_count, col_count)

    conv_local = grads[3].transpose(1, 2, 0, 3).reshape(3, CONV, col_count)
    scale = 1.0 / math.sqrt(row_count * lax.axis_size("ctx"))
    conv_total = summed(conv_local, "ctx") * scale
    return (
        finish(grads[0], rim_back[0]),
        finish(grads[1], rim_back[1]),
        finish(grads[2], rim_back[2]),
        conv_total,
        grads[4],
    )


def solution(mesh):
    return jax.shard_map(
        on_device,
        mesh=mesh,
        in_specs=(
            P("ctx", "head"),
            P("ctx", "head"),
            P("ctx", "head"),
            P(None, None, "head"),
            P("head", "ctx"),
            P("head", None),
            P("ctx", "head"),
        ),
        out_specs=(
            P("ctx", "head"),
            P("ctx", "head"),
            P("ctx", "head"),
            P(None, None, "head"),
            P("head", "ctx"),
        ),
        check_vma=False,
    )
```
